32 devices in a mesh: dp: 8 (over y, x, core), tensor: 4 (over z).
Axes of the slice: x: 2, y: 2, z: 4, core: 2. Of those that a mesh axis runs over, the one named last changes fastest.
Arguments:
- tokens: bfloat16 [8, 2048, 1024], P('dp', 'tensor'), may hold values from -6 to 6
- seg_ids: int32 [8, 2048], P('dp'), may hold values from 0 to 146, never falling along the last dimension, each value on 1 to 15 neighbouring positions
- norm1_gain: float32 [1024], replicated, may hold values from 0.25 to 1.75
- norm1_bias: float32 [1024], replicated, may hold values from -2 to 2
- w_qkv: bfloat16 [1024, 3, 1024], P(None, None, 'tensor'), may hold values from -0.1875 to 0.1875
- w_out: bfloat16 [1024, 1024], P('tensor'), may hold values from -0.5 to 0.5
- norm2_gain: float32 [1024], replicated, may hold values from 0.25 to 1.75
- norm2_bias: float32 [1024], replicated, may hold values from -2 to 2
- w_in: bfloat16 [1024, 2048], P(None, 'tensor'), may hold values from -0.1875 to 0.1875
- w_down: bfloat16 [2048, 1024], P('tensor'), may hold values from -0.125 to 0.125
- cotangent: bfloat16 [8, 2048, 1024], P('dp', 'tensor'), may hold values from -6 to 6
Outputs:
- out_act: bfloat16 [8, 2048, 1024], P('dp', 'tensor')
- grad_tokens: float32 [8, 2048, 1024], P('dp', 'tensor')
- grad_norm1_gain: float32 [1024], replicated
- grad_norm1_bias: float32 [1024], replicated
- grad_qkv: float32 [1024, 3, 1024], P(None, None, 'tensor')
- grad_wout: float32 [1024, 1024], P('tensor')
- grad_norm2_gain: float32 [1024], replicated
- grad_norm2_bias: float32 [1024], replicated
- grad_win: float32 [1024, 2048], P(None, 'tensor')
- grad_wdown: float32 [2048, 1024], P('tensor')
The draws below stay inside these ranges and needn't reach their ends.
Inputs may be any that keep to these rules, and one draw needn't show every extreme that they name: `seg_ids`: within each pack the context numbers never fall, start at 0 and take every value up to 146; each context holds 1 to 15 tokens and one holds exactly 15.
All inputs are finite; a program needn't handle non-finite values.
Results may differ from the reference program's by a relative error of at most 0.019.
Values may be sent and summed in bfloat16 or wider, within the bound.
No kernel may reach another device: no remote copies, remote signals or barrier semaphores. Data moves between devices by JAX's collectives and lax.ppermute only.
A program may use at most 128 MiB of HBM per device.

```python
import math
import jax
import jax.numpy as jnp
import numpy as np
from jax import lax

D = 1024
HEADS = 8
HEAD_DIM = 128
FF = 2048
TOK = 2048
CONTEXT_MAX = 15
CONTEXTS = 147
PACKS = 8
N_TENSOR = 4


def shard_levels(own_key, shape, pieces, low, largest):
    factor_of = 1.0
    for position, shards_of in pieces:
        heights = jax.random.uniform(jax.random.fold_in(jax.random.fold_in(own_key, 6), position), (shards_of,), jnp.float32, low / len(pieces), largest / len(pieces))
        factor_of = factor_of * jnp.repeat(jnp.exp(heights), shape[position] // shards_of).reshape((-1,) + (1,) * (len(shape) - 1 - position))
    return factor_of


def length_profile(amount, total, most, lean):
    portions = [(1 << 20) // math.isqrt(standing ** lean) + 1 for standing in range(2, amount + 1)]
    spare, holding = total - most - (amount - 1), [1] * (amount - 1)
    while spare > 0:
        movable = [i for i in range(amount - 1) if holding[i] < most]
        mass, remaining = sum([portions[i] for i in movable]), spare
        for i in movable:
            addition = min(most - holding[i], max(1, remaining * portions[i] // mass), spare)
            holding[i] = holding[i] + addition
            spare = spare - addition
    return np.array([most] + holding)


def ragged(rng, count, total, limit, lean):
    if count == 2:
        one = jax.random.randint(rng, (), max(1, total - limit), min(limit, total - 1) + 1)
        return jnp.stack([one, total - one])
    sizes = jnp.asarray(length_profile(count, total, limit, lean), jnp.int32)
    couples = (count - 1) // 2
    donor, sink = sizes[1:1 + 2 * couples:2], sizes[2:2 + 2 * couples:2]
    slack = jnp.minimum(donor - 1, limit - sink)
    moved = jax.random.randint(jax.random.fold_in(rng, 1), (couples,), 0, 1 << 20) % (slack + 1)
    sizes = sizes.at[1:1 + 2 * couples:2].set(donor - moved).at[2:2 + 2 * couples:2].set(sink + moved)
    return sizes[jax.random.permutation(jax.random.fold_in(rng, 2), count)]


def centred(key, dims, width, bound, split=(), held_as=jnp.bfloat16):
    array = width * jax.random.normal(key, dims, jnp.float32)
    if split:
        array = array * shard_levels(key, dims, split, -0.22, 0.18)
    return jnp.clip(array, -bound, bound).astype(held_as)


def setup_inputs(seed: int = 0) -> dict:
    key_list = jax.random.split(jax.random.key(seed), 12)
    return {
        "tokens": centred(key_list[0], (PACKS, TOK, D), 1.0, 6.0, ((0, 8), (1, 4))),
        "seg_ids": jax.vmap(lambda own: jnp.searchsorted(jnp.cumsum(ragged(own, CONTEXTS, TOK, CONTEXT_MAX, 0)), jnp.arange(TOK), side="right"))(jax.random.split(key_list[1], PACKS)).reshape((PACKS, TOK)).astype(jnp.int32),
        "norm1_gain": jnp.clip(1.0 + 0.15 * jax.random.normal(key_list[2], (D,), jnp.float32), 0.25, 1.75),
        "norm1_bias": centred(key_list[3], (D,), 0.3, 2.0, (), jnp.float32),
        "w_qkv": centred(key_list[4], (D, 3, D), D ** -0.5, 0.1875, ((2, 4),)),
        "w_out": centred(key_list[5], (D, D), (D // 8) ** -0.5, 0.5, ((0, 4),)),
        "norm2_gain": jnp.clip(1.0 + 0.15 * jax.random.normal(key_list[6], (D,), jnp.float32), 0.25, 1.75),
        "norm2_bias": centred(key_list[7], (D,), 0.3, 2.0, (), jnp.float32),
        "w_in": centred(key_list[8], (D, FF), D ** -0.5, 0.1875, ((1, 4),)),
        "w_down": centred(key_list[9], (FF, D), FF ** -0.5, 0.125, ((0, 4),)),
        "cotangent": centred(key_list[10], (PACKS, TOK, D), 1.0, 6.0, ((0, 8), (1, 4))),
    }


@jax.custom_vjp
def low(v):
    return lax.optimization_barrier(v.astype(jnp.bfloat16)).astype(jnp.float32)

@jax.custom_vjp
def low_back(v):
    return v

def low_keep(v):
    return (low(v), None)

def low_pass(kept, grad):
    return (grad,)

def back_keep(v):
    return (v, None)

def back_low(kept, grad):
    return (low(grad),)
low.defvjp(low_keep, low_pass)
low_back.defvjp(back_keep, back_low)
eps_norm = 1e-05

def layer_norm(values, gain, bias):
    center = values - lax.optimization_barrier(jnp.mean(values, axis=-1, keepdims=True))
    spread = lax.optimization_barrier(jnp.mean(center * center, axis=-1, keepdims=True))
    return center * lax.rsqrt(spread + eps_norm) * gain + bias

def matmul(left, right):
    return jnp.dot(left, right, precision=lax.Precision.HIGHEST)

def pack_forward(rows, segs, params):
    norm1_gain, norm1_bias, w_qkv, w_out, norm2_gain, norm2_bias, w_in, w_down = params
    groups = N_TENSOR
    cols = D // groups
    group_heads = HEADS // groups
    units = FF // groups
    place = jnp.arange(TOK)
    allowed = (segs[:, None] == segs[None, :]) & (place[None, :] <= place[:, None])
    normed1 = low(layer_norm(rows, norm1_gain, norm1_bias))
    attn_total = jnp.zeros((TOK, D), jnp.float32)
    for group in range(groups):
        own_rows = low_back(normed1)
        weight = w_qkv[:, :, group * cols:(group + 1) * cols].reshape(D, 3 * cols)
        packed = matmul(own_rows, weight).reshape(TOK, 3, group_heads, HEAD_DIM)
        queries = low_back(low(packed[:, 0]))
        keys = low_back(low(packed[:, 1]))
        values = low_back(low(packed[:, 2]))
        raw = low_back(jnp.einsum('qhd,khd->hqk', queries, keys, precision=lax.Precision.HIGHEST))
        scores = raw * HEAD_DIM ** (-0.5)
        probs = jax.nn.softmax(jnp.where(allowed[None], scores, -1e+30), axis=-1)
        attended = jnp.einsum('hqk,khd->qhd', low(probs), values, precision=lax.Precision.HIGHEST)
        attended = low_back(low(attended)).reshape(TOK, cols)
        attn_total = attn_total + low(matmul(attended, w_out[group * cols:(group + 1) * cols]))
    mixed = rows + low_back(attn_total)
    normed2 = low(layer_norm(mixed, norm2_gain, norm2_bias))
    ffn_total = jnp.zeros((TOK, D), jnp.float32)
    for group in range(groups):
        own_rows = low_back(normed2)
        pre_act = low_back(matmul(own_rows, w_in[:, group * units:(group + 1) * units]))
        hidden = low(jax.nn.gelu(pre_act, approximate=False))
        ffn_total = ffn_total + low(matmul(hidden, w_down[group * units:(group + 1) * units]))
    return mixed + low_back(ffn_total)

def reference(tokens, seg_ids, norm1_gain, norm1_bias, w_qkv, w_out, norm2_gain, norm2_bias, w_in, w_down, cotangent):
    floats = tuple((item.astype(jnp.float32) for item in (tokens, norm1_gain, norm1_bias, w_qkv, w_out, norm2_gain, norm2_bias, w_in, w_down)))

    def whole(inputs, *params):

        def one_pack(pair):
            return pack_forward(pair[0], pair[1], params)
        return lax.map(jax.checkpoint(one_pack), (inputs, seg_ids))
    result, pullback = jax.vjp(whole, *floats)
    grads = pullback(cotangent.astype(jnp.float32))
    return (result.astype(jnp.bfloat16), grads[0], grads[1], grads[2], grads[3], grads[4], grads[5], grads[6], grads[7], grads[8])
```

```python
import math

import jax
import jax.numpy as jnp
from jax import lax
from jax.sharding import PartitionSpec as P

HEAD_DIM = 128
eps_norm = 1e-05
halo = 16
query_block = 128
ALL = ("dp", "tensor")


def norm_forward(values, gain, bias):
    center = values - jnp.mean(values, axis=-1, keepdims=True)
    spread = jnp.mean(center * center, axis=-1, keepdims=True)
    scaled = lax.rsqrt(spread + eps_norm)
    normal = center * scaled
    return (normal * gain + bias, normal, scaled)


def norm_backward(upstream, normal, scaled, gain):
    weighted = upstream * gain
    inner = (
        weighted
        - jnp.mean(weighted, axis=-1, keepdims=True)
        - normal * jnp.mean(weighted * normal, axis=-1, keepdims=True)
    )
    return (scaled * inner, jnp.sum(upstream * normal, axis=0), jnp.sum(upstream, axis=0))


def gather_groups(shard):
    n_dp = lax.axis_size("dp")
    n_t = lax.axis_size("tensor")
    d = lax.axis_index("dp")
    rows = shard.shape[0] // n_dp
    piece = lax.dynamic_slice_in_dim(shard, d * rows, rows, 0)
    whole = lax.all_gather(piece, ALL, axis=0, tiled=False)
    whole = whole.reshape((n_dp, n_t) + piece.shape)
    whole = jnp.moveaxis(whole, 1, 0)
    return whole.reshape((n_t,) + shard.shape)


def reduce_groups(partial, extra=None):
    n_dp = lax.axis_size("dp")
    n_t, a, b = partial.shape
    pieces = partial.astype(jnp.bfloat16).reshape(n_t, n_dp, a // n_dp, b)
    if extra is not None:
        pieces = jnp.concatenate([pieces, extra.astype(jnp.bfloat16)], axis=2)
    part = lax.psum_scatter(pieces, "dp", scatter_dimension=1, tiled=True)
    part = lax.psum_scatter(part, "tensor", scatter_dimension=0, tiled=True)
    whole = lax.all_gather(part, "dp", axis=1, tiled=True)
    whole = whole.reshape(n_dp, whole.shape[2], b).astype(jnp.float32)
    if extra is None:
        return whole.reshape(a, b), None
    return whole[:, : a // n_dp].reshape(a, b), whole[0, a // n_dp :]


def local(
    tokens,
    seg_ids,
    norm1_gain,
    norm1_bias,
    w_qkv,
    w_out,
    norm2_gain,
    norm2_bias,
    w_in,
    w_down,
    cotangent,
):
    n_t = lax.axis_size("tensor")
    n_dp = lax.axis_size("dp")
    t = lax.axis_index("tensor")
    rows_here = tokens.shape[1]
    width = tokens.shape[2]
    cols = w_qkv.shape[2]
    heads_group = cols // HEAD_DIM
    units = w_in.shape[1]
    scale = HEAD_DIM ** (-0.5)
    nb = rows_here // query_block
    front = query_block - halo
    ext = rows_here + halo

    wqkv_all = gather_groups(w_qkv).reshape(n_t, width, 3 * cols)
    wout_all = gather_groups(w_out)
    win_all = gather_groups(jnp.swapaxes(w_in, 0, 1))
    wdown_all = gather_groups(w_down)

    own = tokens[0]
    prev = lax.ppermute(own[rows_here - halo :], "tensor", [(i, i + 1) for i in range(n_t - 1)])
    rows_ext = jnp.concatenate([prev, own], axis=0).astype(jnp.float32)
    normed1_f, normal1, rstd1 = norm_forward(rows_ext, norm1_gain, norm1_bias)
    normed1 = normed1_f.astype(jnp.bfloat16)

    seg_pack = seg_ids[0]
    seg_pad = jnp.concatenate([jnp.full((query_block,), -1, jnp.int32), seg_pack])
    seg_win = lax.dynamic_slice_in_dim(seg_pad, t * rows_here, rows_here + query_block, 0)
    seg_win = jnp.where(jnp.arange(rows_here + query_block) < front, -1, seg_win)
    seg_blocks = seg_win.reshape(nb + 1, query_block)
    query_segs = seg_blocks[1:]
    key_segs = jnp.concatenate([seg_blocks[:-1], seg_blocks[1:]], axis=1)
    causal = jnp.arange(2 * query_block)[None, :] <= (jnp.arange(query_block)[:, None] + query_block)
    allowed = (query_segs[:, :, None] == key_segs[:, None, :]) & causal[None]

    packed = jnp.einsum("rk,gkn->grn", normed1, wqkv_all, preferred_element_type=jnp.float32)
    packed = packed.astype(jnp.bfloat16)
    queries = packed[:, halo:, :cols].reshape(n_t, nb, query_block, heads_group, HEAD_DIM)

    def windows(part):
        padded = jnp.concatenate([jnp.zeros((n_t, front, cols), jnp.bfloat16), part], axis=1)
        blocks = padded.reshape(n_t, nb + 1, query_block, heads_group, HEAD_DIM)
        return jnp.concatenate([blocks[:, :-1], blocks[:, 1:]], axis=2)

    key_win = windows(packed[:, :, cols : 2 * cols])
    value_win = windows(packed[:, :, 2 * cols :])

    raw = jnp.einsum("gbqhd,gbkhd->gbhqk", queries, key_win, preferred_element_type=jnp.float32)
    masked = jnp.where(allowed[None, :, None], raw * scale, -1e30)
    top = jnp.max(masked, axis=-1, keepdims=True)
    expo = jnp.exp(masked - top)
    probs = expo / jnp.sum(expo, axis=-1, keepdims=True)
    probs_low = probs.astype(jnp.bfloat16)
    attended = jnp.einsum(
        "gbhqk,gbkhd->gbqhd", probs_low, value_win, preferred_element_type=jnp.float32
    ).astype(jnp.bfloat16)
    attended = attended.reshape(n_t, rows_here, cols)

    rows = rows_ext[halo:]
    mixed = rows + jnp.einsum("grc,gcn->rn", attended, wout_all, preferred_element_type=jnp.float32)
    normed2_f, normal2, rstd2 = norm_forward(mixed, norm2_gain, norm2_bias)
    normed2 = normed2_f.astype(jnp.bfloat16)
    pre_act = jnp.einsum("rk,guk->gru", normed2, win_all, preferred_element_type=jnp.float32)
    hidden = jax.nn.gelu(pre_act, approximate=False).astype(jnp.bfloat16)
    final = mixed + jnp.einsum("gru,gun->rn", hidden, wdown_all, preferred_element_type=jnp.float32)
    out_act = final.astype(jnp.bfloat16)[None]

    grad_low = cotangent[0]
    grad_wdown_part = jnp.einsum("gru,rn->gun", hidden, grad_low, preferred_element_type=jnp.float32)
    grad_hidden = jnp.einsum("rn,gun->gru", grad_low, wdown_all, preferred_element_type=jnp.float32)
    cdf = 0.5 * (1.0 + lax.erf(pre_act * (1.0 / math.sqrt(2.0))))
    pdf = jnp.exp(-0.5 * pre_act * pre_act) * (1.0 / math.sqrt(2.0 * math.pi))
    grad_pre = (grad_hidden * (cdf + pre_act * pdf)).astype(jnp.bfloat16)
    grad_win_part = jnp.einsum("rk,gru->guk", normed2, grad_pre, preferred_element_type=jnp.float32)
    grad_normed2 = jnp.einsum("gru,guk->rk", grad_pre, win_all, preferred_element_type=jnp.float32)
    grad_back2, grad_gain2, grad_bias2 = norm_backward(grad_normed2, normal2, rstd2, norm2_gain)
    grad_mixed = grad_low.astype(jnp.float32) + grad_back2
    mixed_low = grad_mixed.astype(jnp.bfloat16)
    grad_wout_part = jnp.einsum("grc,rn->gcn", attended, mixed_low, preferred_element_type=jnp.float32)
    grad_att = jnp.einsum("rn,gcn->grc", mixed_low, wout_all, preferred_element_type=jnp.float32)
    grad_att = grad_att.astype(jnp.bfloat16).reshape(n_t, nb, query_block, heads_group, HEAD_DIM)

    grad_prob = jnp.einsum("gbqhd,gbkhd->gbhqk", grad_att, value_win, preferred_element_type=jnp.float32)
    inner = jnp.sum(probs * grad_prob, axis=-1, keepdims=True)
    grad_raw = jnp.where(allowed[None, :, None], probs * (grad_prob - inner) * scale, 0.0)
    grad_raw = grad_raw.astype(jnp.bfloat16)
    grad_q = jnp.einsum("gbhqk,gbkhd->gbqhd", grad_raw, key_win, preferred_element_type=jnp.float32)
    grad_kw = jnp.einsum("gbhqk,gbqhd->gbkhd", grad_raw, queries, preferred_element_type=jnp.float32)
    grad_vw = jnp.einsum("gbhqk,gbqhd->gbkhd", probs_low, grad_att, preferred_element_type=jnp.float32)

    def unwindow(grad_w):
        first = jnp.pad(grad_w[:, :, :query_block], ((0, 0), (0, 1), (0, 0), (0, 0), (0, 0)))
        second = jnp.pad(grad_w[:, :, query_block:], ((0, 0), (1, 0), (0, 0), (0, 0), (0, 0)))
        summed = (first + second).reshape(n_t, (nb + 1) * query_block, cols)
        return summed[:, front:]

    grad_q = jnp.concatenate(
        [jnp.zeros((n_t, halo, cols), jnp.float32), grad_q.reshape(n_t, rows_here, cols)], axis=1
    )
    grad_proj = jnp.concatenate([grad_q, unwindow(grad_kw), unwindow(grad_vw)], axis=2)
    grad_proj = grad_proj.astype(jnp.bfloat16)
    grad_qkv_part = jnp.einsum("rk,grn->gkn", normed1, grad_proj, preferred_element_type=jnp.float32)
    grad_normed1 = jnp.einsum("grn,gkn->rk", grad_proj, wqkv_all, preferred_element_type=jnp.float32)
    back = lax.ppermute(grad_normed1[:halo], "tensor", [(i + 1, i) for i in range(n_t - 1)])
    grad_normed1 = grad_normed1[halo:] + jnp.pad(back, ((rows_here - halo, 0), (0, 0)))
    grad_back1, grad_gain1, grad_bias1 = norm_backward(
        grad_normed1, normal1[halo:], rstd1[halo:], norm1_gain
    )
    grad_tokens = (grad_mixed + grad_back1)[None]

    norm_total = lax.psum(jnp.stack([grad_gain1, grad_bias1, grad_gain2, grad_bias2]), ALL)
    grad_wdown, _ = reduce_groups(grad_wdown_part)
    grad_win, _ = reduce_groups(grad_win_part)
    grad_wout, _ = reduce_groups(grad_wout_part)
    grad_qkv, _ = reduce_groups(grad_qkv_part)
    return (
        out_act,
        grad_tokens,
        norm_total[0],
        norm_total[1],
        grad_qkv.reshape(width, 3, cols),
        grad_wout,
        norm_total[2],
        norm_total[3],
        jnp.swapaxes(grad_win, 0, 1),
        grad_wdown,
    )


def solution(mesh):
    return jax.shard_map(
        local,
        mesh=mesh,
        in_specs=(
            P("dp", "tensor", None),
            P("dp", None),
            P(),
            P(),
            P(None, None, "tensor"),
            P("tensor", None),
            P(),
            P(),
            P(None, "tensor"),
            P("tensor", None),
            P("dp", "tensor", None),
        ),
        out_specs=(
            P("dp", "tensor", None),
            P("dp", "tensor", None),
            P(),
            P(),
            P(None, None, "tensor"),
            P("tensor", None),
            P(),
            P(),
            P(None, "tensor"),
            P("tensor", None),
        ),
        check_vma=False,
    )
```
